1024 devices in a mesh: dp: 16 (over y, z_hi), gz: 64 (over x, z_lo, core).
Axes of the slice: x: 4, y: 8, z: 16 (z_hi: 2, z_lo: 8; z = z_hi * 8 + z_lo), core: 2. Of those that a mesh axis runs over, the one named last changes fastest.
Arguments:
- volume: bfloat16 [64, 16, 16, 2048], P('gz', 'dp'), may hold values from -6 to 6
- weight: bfloat16 [1728, 64], replicated, may hold values from -0.15625 to 0.15625
- cotangent: bfloat16 [64, 16, 16, 2048], P('gz', 'dp'), may hold values from -6 to 6
Outputs:
- activation: bfloat16 [64, 16, 16, 2048], P('gz', 'dp')
- input_grad: bfloat16 [64, 16, 16, 2048], P('gz', 'dp')
- weight_grad: float32 [1728, 64], P('gz', 'dp')
The draws below stay inside these ranges and needn't reach their ends.
All inputs are finite; a program needn't handle non-finite values.
Results may differ from the reference program's by a relative error of at most 0.01.
Values may be sent and summed in bfloat16 or wider, within the bound.
No kernel may reach another device: no remote copies, remote signals or barrier semaphores. Data moves between devices by JAX's collectives and lax.ppermute only.
A program may use at most 32 MiB of HBM per device.

```python
import math
import jax
import jax.numpy as jnp
from jax import lax

C = 64
NH = 16
NW = 32
UNIVERSES = 64
NZ = 16


def levels(key, dims, cuts, least, top_value):
    loudness, own = 1.0, jax.random.fold_in(key, 6)
    for axis_at, parts in cuts:
        heights = jnp.exp(jax.random.uniform(jax.random.fold_in(own, axis_at), (parts,), jnp.float32, least / len(cuts), top_value / len(cuts)))
        loudness = loudness * jnp.repeat(heights, dims[axis_at] // parts).reshape([-1 if axis == axis_at else 1 for axis in range(len(dims))])
    return loudness


def scatter_about(stream_key, dims, width, limit, shards=(), held_as=jnp.bfloat16):
    drawn = jax.random.normal(stream_key, dims, jnp.float32) * width
    if len(shards) > 0:
        drawn = levels(stream_key, dims, shards, -0.22, 0.18) * drawn
    return jnp.clip(drawn, min=-limit, max=limit).astype(held_as)


def setup_inputs(seed: int = 0) -> dict:
    splits = jax.random.split(jax.random.key(seed), 4)
    volume = scatter_about(splits[0], (UNIVERSES, NZ, NH, NW * C), 1.0, 6.0, ((0, 64), (1, 16)))
    weight = scatter_about(splits[1], (27 * C, C), (27 * C) ** -0.5, 0.15625)
    cotangent = scatter_about(splits[2], (UNIVERSES, NZ, NH, NW * C), 1.0, 6.0, ((0, 64), (1, 16)))
    return {"volume": volume, "weight": weight, "cotangent": cotangent}


def reference(volume, weight, cotangent):
    kern = weight.astype(jnp.float32).reshape(3, 3, 3, C, C)
    hp = lax.Precision.HIGHEST

    def one_universe(pair):
        vol, cot = pair
        grid = vol.astype(jnp.float32).reshape(NZ, NH, NW, C)
        padded = jnp.pad(grid, ((1, 1), (1, 1), (1, 1), (0, 0)))
        pre = jnp.zeros((NZ * NH * NW, C), jnp.float32)
        for a in range(3):
            for b in range(3):
                for c in range(3):
                    window = padded[a:a + NZ, b:b + NH, c:c + NW].reshape(NZ * NH * NW, C)
                    pre = pre + jnp.dot(window, kern[a, b, c], precision=hp)
        sig = jax.nn.sigmoid(pre)
        act = (pre * sig).astype(jnp.bfloat16)
        delta_low = lax.optimization_barrier((cot.astype(jnp.float32).reshape(NZ * NH * NW, C) * sig * (1.0 + pre * (1.0 - sig))).astype(jnp.bfloat16))
        delta = delta_low.astype(jnp.float32)
        dpad = jnp.pad(delta.reshape(NZ, NH, NW, C), ((1, 1), (1, 1), (1, 1), (0, 0)))
        back = jnp.zeros((NZ * NH * NW, C), jnp.float32)
        grads = []
        for a in range(3):
            for b in range(3):
                for c in range(3):
                    window = dpad[2 - a:2 - a + NZ, 2 - b:2 - b + NH, 2 - c:2 - c + NW].reshape(NZ * NH * NW, C)
                    back = back + jnp.dot(window, kern[a, b, c].T, precision=hp)
                    source = padded[a:a + NZ, b:b + NH, c:c + NW].reshape(NZ * NH * NW, C)
                    grads.append(jnp.dot(source.T, delta, precision=hp))
        return (act.reshape(NZ, NH, NW * C), back.astype(jnp.bfloat16).reshape(NZ, NH, NW * C), jnp.stack(grads, 0))
    activation, input_grad, partial_grads = lax.map(one_universe, (volume, cotangent))
    scale = 1.0 / math.sqrt(UNIVERSES * NZ * NH * NW)
    weight_grad = lax.optimization_barrier(jnp.sum(partial_grads, 0)).reshape(27 * C, C) * scale
    return (activation, input_grad, weight_grad)
```

```python
import math

import jax
import jax.numpy as jnp
from jax import lax
from jax.sharding import PartitionSpec as P


def padded_2(block, sides, width):
    for axis, dim in sides:
        count = lax.axis_size(axis)
        forward = [(i, i + 1) for i in range(count - 1)]
        backward = [(target, source) for source, target in forward]
        low = lax.ppermute(
            lax.slice_in_dim(block, block.shape[dim] - width, None, axis=dim), axis, forward
        )
        high = lax.ppermute(lax.slice_in_dim(block, 0, width, axis=dim), axis, backward)
        block = jnp.concatenate([low, block, high], axis=dim)
    return block


def split_up(value, dim, size):
    dims = value.shape
    pieces = value.reshape(*dims[:dim], size, dims[dim] // size, *dims[dim + 1 :])
    return jnp.moveaxis(pieces, dim, 0)


def sum_at_owner(value, axis, dim):
    size = lax.axis_size(axis)
    pieces = lax.all_to_all(split_up(value, dim, size), axis, 0, 0, tiled=True)
    return jnp.sum(pieces.astype(jnp.float32), axis=0)


def sum_at_owner_2(value, axis, dim):
    pieces = split_up(value, dim, lax.axis_size(axis))
    arrived = lax.all_to_all(pieces, axis, split_axis=0, concat_axis=0, tiled=True)
    return arrived.sum(axis=0)


def strips(padded, z_start, y_start, planes, height, width, order):
    parts = [
        padded[z_start : z_start + planes, y_start : y_start + height, x_start : x_start + width]
        for x_start in order
    ]
    joined = jnp.concatenate(parts, axis=-1)
    return joined.reshape(planes * height * width, joined.shape[-1])


def halo_planes(block, axis, depth):
    count = lax.axis_size(axis)
    planes = block.shape[1]
    below, above = [], []
    for shift in range(1, -(-depth // planes) + 1):
        forward = [(i, i + shift) for i in range(count - shift)]
        backward = [(target, source) for source, target in forward]
        below.insert(0, lax.ppermute(block, axis, forward))
        above.append(lax.ppermute(block, axis, backward))
    low = jnp.concatenate(below, axis=1)
    high = jnp.concatenate(above, axis=1)
    low = lax.slice_in_dim(low, low.shape[1] - depth, None, axis=1)
    high = lax.slice_in_dim(high, 0, depth, axis=1)
    return low, high


def per_device(volume, weight, cotangent):
    chans = weight.shape[1]
    planes = volume.shape[1]
    height = volume.shape[2]
    width = volume.shape[3] // chans
    cells = planes * height * width
    both = jnp.concatenate([volume, cotangent], axis=0)
    low1, high1 = halo_planes(both, "dp", 1)
    low2, high2 = halo_planes(volume, "dp", 2)
    v_ext = jnp.concatenate([low2[:, :1], low1[:1], volume, high1[:1], high2[:, 1:]], axis=1)
    c_ext = jnp.concatenate([low1[1:], cotangent, high1[1:]], axis=1)
    ext = planes + 2
    padded = jnp.pad(
        v_ext.reshape(planes + 4, height, width, chans), ((0, 0), (1, 1), (1, 1), (0, 0))
    )
    blocks = []
    flipped = []
    for tap_z in range(3):
        for tap_y in range(3):
            first = (tap_z * 3 + tap_y) * 3 * chans
            block = weight[first : first + 3 * chans]
            blocks.append(block)
            flipped.append(
                block.reshape(3, chans, chans).transpose(0, 2, 1).reshape(3 * chans, chans)
            )
    pre = jnp.zeros((ext * height * width, chans), jnp.float32)
    for tap_z in range(3):
        for tap_y in range(3):
            window = strips(padded, tap_z, tap_y, ext, height, width, (0, 1, 2))
            pre = pre + jnp.dot(
                window, blocks[tap_z * 3 + tap_y], preferred_element_type=jnp.float32
            )
    sig = jax.nn.sigmoid(pre)
    inner = slice(height * width, (planes + 1) * height * width)
    activation = (pre[inner] * sig[inner]).astype(jnp.bfloat16)
    activation = activation.reshape(1, planes, height, width * chans)
    delta_ext = (
        c_ext.reshape(ext * height * width, chans).astype(jnp.float32)
        * sig
        * (1.0 + pre * (1.0 - sig))
    ).astype(jnp.bfloat16)
    delta = delta_ext[inner]
    delta_pad = jnp.pad(
        delta_ext.reshape(ext, height, width, chans), ((0, 0), (1, 1), (1, 1), (0, 0))
    )
    back = jnp.zeros((cells, chans), jnp.float32)
    for tap_z in range(3):
        for tap_y in range(3):
            window = strips(delta_pad, 2 - tap_z, 2 - tap_y, planes, height, width, (2, 1, 0))
            back = back + jnp.dot(
                window, flipped[tap_z * 3 + tap_y], preferred_element_type=jnp.float32
            )
    summed = back.reshape(planes, height, width * chans)
    input_grad = summed.astype(jnp.bfloat16).reshape(1, planes, height, width * chans)
    pieces = []
    for tap_z in range(3):
        for tap_y in range(3):
            window = strips(padded, 1 + tap_z, tap_y, planes, height, width, (0, 1, 2))
            pieces.append(
                lax.dot_general(
                    window, delta, (((0,), (0,)), ((), ())), preferred_element_type=jnp.float32
                )
            )
    scale = 1.0 / math.sqrt(lax.axis_size("dp") * lax.axis_size("gz") * cells)
    terms = jnp.concatenate(pieces, axis=0) * scale
    reduced = sum_at_owner(terms.astype(jnp.bfloat16), "dp", 1)
    weight_grad = sum_at_owner_2(reduced, "gz", 0)
    return (activation, input_grad, weight_grad)


def solution(mesh):
    return jax.shard_map(
        per_device,
        mesh=mesh,
        in_specs=(P("gz", "dp", None, None), P(), P("gz", "dp", None, None)),
        out_specs=(P("gz", "dp", None, None), P("gz", "dp", None, None), P("gz", "dp")),
        check_vma=False,
    )
```

```python
import math

import jax
import jax.numpy as jnp
from jax import lax
from jax.sharding import PartitionSpec as P


def padded_2(block, sides, width):
    for axis, dim in sides:
        count = lax.axis_size(axis)
        forward = [(i, i + 1) for i in range(count - 1)]
        backward = [(target, source) for source, target in forward]
        low = lax.ppermute(
            lax.slice_in_dim(block, block.shape[dim] - width, None, axis=dim), axis, forward
        )
        high = lax.ppermute(lax.slice_in_dim(block, 0, width, axis=dim), axis, backward)
        block = jnp.concatenate([low, block, high], axis=dim)
    return block


def split_up(value, dim, size):
    dims = value.shape
    pieces = value.reshape(*dims[:dim], size, dims[dim] // size, *dims[dim + 1 :])
    return jnp.moveaxis(pieces, dim, 0)


def sum_at_owner(value, axis, dim):
    size = lax.axis_size(axis)
    pieces = lax.all_to_all(split_up(value, dim, size), axis, 0, 0, tiled=True)
    return jnp.sum(pieces.astype(jnp.float32), axis=0)


def sum_at_owner_2(value, axis, dim):
    pieces = split_up(value, dim, lax.axis_size(axis))
    arrived = lax.all_to_all(pieces, axis, split_axis=0, concat_axis=0, tiled=True)
    return arrived.sum(axis=0)


def strips(padded, z_start, y_start, planes, height, width, order):
    parts = [
        padded[z_start : z_start + planes, y_start : y_start + height, x_start : x_start + width]
        for x_start in order
    ]
    joined = jnp.concatenate(parts, axis=-1)
    return joined.reshape(planes * height * width, joined.shape[-1])


def per_device(volume, weight, cotangent):
    chans = weight.shape[1]
    planes = volume.shape[1]
    height = volume.shape[2]
    width = volume.shape[3] // chans
    cells = planes * height * width
    kern = weight.reshape(3, 3, 3, chans, chans)
    dims = ("NDHWC", "DHWIO", "NDHWC")
    same = [(0, 0), (1, 1), (1, 1)]
    extended = padded_2(volume, (("dp", 1),), 1)
    v_ext = extended.reshape(1, planes + 2, height, width, chans)
    pre = lax.conv_general_dilated(
        v_ext, kern, (1, 1, 1), same, dimension_numbers=dims, preferred_element_type=jnp.float32
    ).reshape(cells, chans)
    sig = jax.nn.sigmoid(pre)
    activation = (pre * sig).astype(jnp.bfloat16).reshape(1, planes, height, width * chans)
    delta = (
        cotangent.reshape(cells, chans).astype(jnp.float32) * sig * (1.0 + pre * (1.0 - sig))
    ).astype(jnp.bfloat16)
    delta_ext = padded_2(delta.reshape(1, planes, height, width * chans), (("dp", 1),), 1)
    d_ext = delta_ext.reshape(1, planes + 2, height, width, chans)
    flipped = jnp.flip(kern, (0, 1, 2)).transpose(0, 1, 2, 4, 3)
    back = lax.conv_general_dilated(
        d_ext, flipped, (1, 1, 1), same, dimension_numbers=dims, preferred_element_type=jnp.float32
    )
    input_grad = back.astype(jnp.bfloat16).reshape(1, planes, height, width * chans)
    v_pad = jnp.pad(v_ext, ((0, 0), (0, 0), (1, 1), (1, 1), (0, 0)))
    grads = lax.conv_general_dilated(
        v_pad,
        delta.reshape(1, planes, height, width, chans),
        (1, 1, 1),
        [(0, 0), (0, 0), (0, 0)],
        dimension_numbers=("CDHWN", "IDHWO", "NDHWC"),
        preferred_element_type=jnp.float32,
    )
    scale = 1.0 / math.sqrt(lax.axis_size("dp") * lax.axis_size("gz") * cells)
    terms = grads.transpose(1, 2, 3, 0, 4).reshape(27 * chans, chans) * scale
    reduced = sum_at_owner(terms.astype(jnp.bfloat16), "dp", 1)
    weight_grad = sum_at_owner_2(reduced, "gz", 0)
    return (activation, input_grad, weight_grad)


def solution(mesh):
    return jax.shard_map(
        per_device,
        mesh=mesh,
        in_specs=(P("gz", "dp", None, None), P(), P("gz", "dp", None, None)),
        out_specs=(P("gz", "dp", None, None), P("gz", "dp", None, None), P("gz", "dp")),
        check_vma=False,
    )
```

```python
import math

import jax
import jax.numpy as jnp
from jax import lax
from jax.sharding import PartitionSpec as P


def padded_2(block, sides, width):
    for axis, dim in sides:
        count = lax.axis_size(axis)
        forward = [(i, i + 1) for i in range(count - 1)]
        backward = [(target, source) for source, target in forward]
        low = lax.ppermute(
            lax.slice_in_dim(block, block.shape[dim] - width, None, axis=dim), axis, forward
        )
        high = lax.ppermute(lax.slice_in_dim(block, 0, width, axis=dim), axis, backward)
        block = jnp.concatenate([low, block, high], axis=dim)
    return block


def split_up(value, dim, size):
    dims = value.shape
    pieces = value.reshape(*dims[:dim], size, dims[dim] // size, *dims[dim + 1 :])
    return jnp.moveaxis(pieces, dim, 0)


def sum_at_owner(value, axis, dim):
    size = lax.axis_size(axis)
    pieces = lax.all_to_all(split_up(value, dim, size), axis, 0, 0, tiled=True)
    return jnp.sum(pieces.astype(jnp.float32), axis=0)


def sum_at_owner_2(value, axis, dim):
    pieces = split_up(value, dim, lax.axis_size(axis))
    arrived = lax.all_to_all(pieces, axis, split_axis=0, concat_axis=0, tiled=True)
    return arrived.sum(axis=0)


def strips(padded, z_start, y_start, planes, height, width, order):
    parts = [
        padded[z_start : z_start + planes, y_start : y_start + height, x_start : x_start + width]
        for x_start in order
    ]
    joined = jnp.concatenate(parts, axis=-1)
    return joined.reshape(planes * height * width, joined.shape[-1])


def halo_planes(block, axis, depth):
    count = lax.axis_size(axis)
    planes = block.shape[1]
    below, above = [], []
    for shift in range(1, -(-depth // planes) + 1):
        forward = [(i, i + shift) for i in range(count - shift)]
        backward = [(target, source) for source, target in forward]
        below.insert(0, lax.ppermute(block, axis, forward))
        above.append(lax.ppermute(block, axis, backward))
    low = jnp.concatenate(below, axis=1)
    high = jnp.concatenate(above, axis=1)
    low = lax.slice_in_dim(low, low.shape[1] - depth, None, axis=1)
    high = lax.slice_in_dim(high, 0, depth, axis=1)
    return low, high


def per_device(volume, weight, cotangent):
    chans = weight.shape[1]
    planes = volume.shape[1]
    height = volume.shape[2]
    width = volume.shape[3] // chans
    cells = planes * height * width
    ext = planes + 2
    kern = weight.reshape(3, 3, 3, chans, chans)
    dims = ("NDHWC", "DHWIO", "NDHWC")
    same = [(0, 0), (1, 1), (1, 1)]
    both = jnp.concatenate([volume, cotangent], axis=0)
    low1, high1 = halo_planes(both, "dp", 1)
    low2, high2 = halo_planes(volume, "dp", 2)
    v_ext = jnp.concatenate([low2[:, :1], low1[:1], volume, high1[:1], high2[:, 1:]], axis=1)
    c_ext = jnp.concatenate([low1[1:], cotangent, high1[1:]], axis=1)
    v_ext = v_ext.reshape(1, planes + 4, height, width, chans)
    pre = lax.conv_general_dilated(
        v_ext, kern, (1, 1, 1), same, dimension_numbers=dims, preferred_element_type=jnp.float32
    ).reshape(ext * height * width, chans)
    sig = jax.nn.sigmoid(pre)
    inner = slice(height * width, (planes + 1) * height * width)
    activation = (pre[inner] * sig[inner]).astype(jnp.bfloat16)
    activation = activation.reshape(1, planes, height, width * chans)
    delta_ext = (
        c_ext.reshape(ext * height * width, chans).astype(jnp.float32)
        * sig
        * (1.0 + pre * (1.0 - sig))
    ).astype(jnp.bfloat16)
    delta = delta_ext[inner]
    d_ext = delta_ext.reshape(1, ext, height, width, chans)
    flipped = jnp.flip(kern, (0, 1, 2)).transpose(0, 1, 2, 4, 3)
    back = lax.conv_general_dilated(
        d_ext, flipped, (1, 1, 1), same, dimension_numbers=dims, preferred_element_type=jnp.float32
    )
    input_grad = back.astype(jnp.bfloat16).reshape(1, planes, height, width * chans)
    v_pad = jnp.pad(v_ext[:, 1 : 1 + ext], ((0, 0), (0, 0), (1, 1), (1, 1), (0, 0)))
    grads = lax.conv_general_dilated(
        v_pad,
        delta.reshape(1, planes, height, width, chans),
        (1, 1, 1),
        [(0, 0), (0, 0), (0, 0)],
        dimension_numbers=("CDHWN", "IDHWO", "NDHWC"),
        preferred_element_type=jnp.float32,
    )
    scale = 1.0 / math.sqrt(lax.axis_size("dp") * lax.axis_size("gz") * cells)
    terms = grads.transpose(1, 2, 3, 0, 4).reshape(27 * chans, chans) * scale
    reduced = sum_at_owner(terms.astype(jnp.bfloat16), "dp", 1)
    weight_grad = sum_at_owner_2(reduced, "gz", 0)
    return (activation, input_grad, weight_grad)


def solution(mesh):
    return jax.shard_map(
        per_device,
        mesh=mesh,
        in_specs=(P("gz", "dp", None, None), P(), P("gz", "dp", None, None)),
        out_specs=(P("gz", "dp", None, None), P("gz", "dp", None, None), P("gz", "dp")),
        check_vma=False,
    )
```

```python
import math

import jax
import jax.numpy as jnp
from jax import lax
from jax.sharding import PartitionSpec as P


def padded_2(block, sides, width):
    for axis, dim in sides:
        count = lax.axis_size(axis)
        forward = [(i, i + 1) for i in range(count - 1)]
        backward = [(target, source) for source, target in forward]
        low = lax.ppermute(
            lax.slice_in_dim(block, block.shape[dim] - width, None, axis=dim), axis, forward
        )
        high = lax.ppermute(lax.slice_in_dim(block, 0, width, axis=dim), axis, backward)
        block = jnp.concatenate([low, block, high], axis=dim)
    return block


def split_up(value, dim, size):
    dims = value.shape
    pieces = value.reshape(*dims[:dim], size, dims[dim] // size, *dims[dim + 1 :])
    return jnp.moveaxis(pieces, dim, 0)


def sum_at_owner(value, axis, dim):
    size = lax.axis_size(axis)
    pieces = lax.all_to_all(split_up(value, dim, size), axis, 0, 0, tiled=True)
    return jnp.sum(pieces.astype(jnp.float32), axis=0)


def sum_at_owner_2(value, axis, dim):
    pieces = split_up(value, dim, lax.axis_size(axis))
    arrived = lax.all_to_all(pieces, axis, split_axis=0, concat_axis=0, tiled=True)
    return arrived.sum(axis=0)


def strips(padded, z_start, y_start, planes, height, width, order):
    parts = [
        padded[z_start : z_start + planes, y_start : y_start + height, x_start : x_start + width]
        for x_start in order
    ]
    joined = jnp.concatenate(parts, axis=-1)
    return joined.reshape(planes * height * width, joined.shape[-1])


def per_device(volume, weight, cotangent):
    chans = weight.shape[1]
    planes = volume.shape[1]
    height = volume.shape[2]
    width = volume.shape[3] // chans
    cells = planes * height * width
    kern = weight.reshape(3, 3, 3, chans, chans)
    dims = ("NDHWC", "DHWIO", "NDHWC")
    same = [(0, 0), (1, 1), (1, 1)]
    extended = padded_2(volume, (("dp", 1),), 1)
    v_ext = extended.reshape(1, planes + 2, height, width, chans)
    pre = lax.conv_general_dilated(
        v_ext, kern, (1, 1, 1), same, dimension_numbers=dims, preferred_element_type=jnp.float32
    ).reshape(cells, chans)
    sig = jax.nn.sigmoid(pre)
    activation = (pre * sig).astype(jnp.bfloat16).reshape(1, planes, height, width * chans)
    delta = (
        cotangent.reshape(cells, chans).astype(jnp.float32) * sig * (1.0 + pre * (1.0 - sig))
    ).astype(jnp.bfloat16)
    delta_ext = padded_2(delta.reshape(1, planes, height, width * chans), (("dp", 1),), 1)
    d_ext = delta_ext.reshape(1, planes + 2, height, width, chans)
    flipped = jnp.flip(kern, (0, 1, 2)).transpose(0, 1, 2, 4, 3)
    back = lax.conv_general_dilated(
        d_ext, flipped, (1, 1, 1), same, dimension_numbers=dims, preferred_element_type=jnp.float32
    )
    input_grad = back.astype(jnp.bfloat16).reshape(1, planes, height, width * chans)
    v_pad = jnp.pad(v_ext, ((0, 0), (0, 0), (1, 1), (1, 1), (0, 0)))
    grads = lax.conv_general_dilated(
        v_pad,
        delta.reshape(1, planes, height, width, chans),
        (1, 1, 1),
        [(0, 0), (0, 0), (0, 0)],
        dimension_numbers=("CDHWN", "IDHWO", "NDHWC"),
        preferred_element_type=jnp.float32,
    )
    scale = 1.0 / math.sqrt(lax.axis_size("dp") * lax.axis_size("gz") * cells)
    terms = grads.transpose(1, 2, 3, 0, 4).reshape(27 * chans, chans) * scale
    gsz, dsz = lax.axis_size("gz"), lax.axis_size("dp")
    rows, cols = terms.shape
    arranged = terms.astype(jnp.bfloat16).reshape(gsz, rows // gsz, dsz, cols // dsz)
    arranged = arranged.transpose(0, 2, 1, 3).reshape(gsz * dsz, rows // gsz, cols // dsz)
    arrived = lax.all_to_all(arranged, ("gz", "dp"), 0, 0, tiled=True)
    weight_grad = jnp.sum(arrived.astype(jnp.float32), axis=0)
    return (activation, input_grad, weight_grad)


def solution(mesh):
    return jax.shard_map(
        per_device,
        mesh=mesh,
        in_specs=(P("gz", "dp", None, None), P(), P("gz", "dp", None, None)),
        out_specs=(P("gz", "dp", None, None), P("gz", "dp", None, None), P("gz", "dp")),
        check_vma=False,
    )
```

```python
import math

import jax
import jax.numpy as jnp
from jax import lax
from jax.sharding import PartitionSpec as P


def padded_2(block, sides, width):
    for axis, dim in sides:
        count = lax.axis_size(axis)
        forward = [(i, i + 1) for i in range(count - 1)]
        backward = [(target, source) for source, target in forward]
        low = lax.ppermute(
            lax.slice_in_dim(block, block.shape[dim] - width, None, axis=dim), axis, forward
        )
        high = lax.ppermute(lax.slice_in_dim(block, 0, width, axis=dim), axis, backward)
        block = jnp.concatenate([low, block, high], axis=dim)
    return block


def split_up(value, dim, size):
    dims = value.shape
    pieces = value.reshape(*dims[:dim], size, dims[dim] // size, *dims[dim + 1 :])
    return jnp.moveaxis(pieces, dim, 0)


def sum_at_owner(value, axis, dim):
    size = lax.axis_size(axis)
    pieces = lax.all_to_all(split_up(value, dim, size), axis, 0, 0, tiled=True)
    return jnp.sum(pieces.astype(jnp.float32), axis=0)


def sum_at_owner_2(value, axis, dim):
    pieces = split_up(value, dim, lax.axis_size(axis))
    arrived = lax.all_to_all(pieces, axis, split_axis=0, concat_axis=0, tiled=True)
    return arrived.sum(axis=0)


def strips(padded, z_start, y_start, planes, height, width, order):
    parts = [
        padded[z_start : z_start + planes, y_start : y_start + height, x_start : x_start + width]
        for x_start in order
    ]
    joined = jnp.concatenate(parts, axis=-1)
    return joined.reshape(planes * height * width, joined.shape[-1])


def per_device(volume, weight, cotangent):
    chans = weight.shape[1]
    planes = volume.shape[1]
    height = volume.shape[2]
    width = volume.shape[3] // chans
    cells = planes * height * width
    kern = weight.reshape(3, 3, 3, chans, chans)
    dims = ("NDHWC", "DHWIO", "NDHWC")
    same = [(0, 0), (1, 1), (1, 1)]
    extended = padded_2(volume, (("dp", 1),), 1)
    v_ext = extended.reshape(1, planes + 2, height, width, chans)
    pre = lax.conv_general_dilated(
        v_ext, kern, (1, 1, 1), same, dimension_numbers=dims, preferred_element_type=jnp.float32
    ).reshape(cells, chans)
    sig = jax.nn.sigmoid(pre)
    activation = (pre * sig).astype(jnp.bfloat16).reshape(1, planes, height, width * chans)
    delta = (
        cotangent.reshape(cells, chans).astype(jnp.float32) * sig * (1.0 + pre * (1.0 - sig))
    ).astype(jnp.bfloat16)
    delta_ext = padded_2(delta.reshape(1, planes, height, width * chans), (("dp", 1),), 1)
    d_ext = delta_ext.reshape(1, planes + 2, height, width, chans)
    flipped = jnp.flip(kern, (0, 1, 2)).transpose(0, 1, 2, 4, 3)
    back = lax.conv_general_dilated(
        d_ext, flipped, (1, 1, 1), same, dimension_numbers=dims, preferred_element_type=jnp.float32
    )
    input_grad = back.astype(jnp.bfloat16).reshape(1, planes, height, width * chans)
    v_pad = jnp.pad(v_ext, ((0, 0), (0, 0), (1, 1), (1, 1), (0, 0)))
    grads = lax.conv_general_dilated(
        v_pad,
        delta.reshape(1, planes, height, width, chans),
        (1, 1, 1),
        [(0, 0), (0, 0), (0, 0)],
        dimension_numbers=("CDHWN", "IDHWO", "NDHWC"),
        preferred_element_type=jnp.float32,
    )
    scale = 1.0 / math.sqrt(lax.axis_size("dp") * lax.axis_size("gz") * cells)
    terms = grads.transpose(1, 2, 3, 0, 4).reshape(27 * chans, chans) * scale
    reduced = sum_at_owner(terms.astype(jnp.bfloat16), "gz", 0)
    weight_grad = sum_at_owner_2(reduced, "dp", 1)
    return (activation, input_grad, weight_grad)


def solution(mesh):
    return jax.shard_map(
        per_device,
        mesh=mesh,
        in_specs=(P("gz", "dp", None, None), P(), P("gz", "dp", None, None)),
        out_specs=(P("gz", "dp", None, None), P("gz", "dp", None, None), P("gz", "dp")),
        check_vma=False,
    )
```

```python
import math

import jax
import jax.numpy as jnp
from jax import lax
from jax.sharding import PartitionSpec as P


def padded_2(block, sides, width):
    for axis, dim in sides:
        count = lax.axis_size(axis)
        forward = [(i, i + 1) for i in range(count - 1)]
        backward = [(target, source) for source, target in forward]
        low = lax.ppermute(
            lax.slice_in_dim(block, block.shape[dim] - width, None, axis=dim), axis, forward
        )
        high = lax.ppermute(lax.slice_in_dim(block, 0, width, axis=dim), axis, backward)
        block = jnp.concatenate([low, block, high], axis=dim)
    return block


def split_up(value, dim, size):
    dims = value.shape
    pieces = value.reshape(*dims[:dim], size, dims[dim] // size, *dims[dim + 1 :])
    return jnp.moveaxis(pieces, dim, 0)


def sum_at_owner(value, axis, dim):
    size = lax.axis_size(axis)
    pieces = lax.all_to_all(split_up(value, dim, size), axis, 0, 0, tiled=True)
    return jnp.sum(pieces.astype(jnp.float32), axis=0)


def sum_at_owner_2(value, axis, dim):
    pieces = split_up(value, dim, lax.axis_size(axis))
    arrived = lax.all_to_all(pieces, axis, split_axis=0, concat_axis=0, tiled=True)
    return arrived.sum(axis=0)


def strips(padded, z_start, y_start, planes, height, width, order):
    parts = [
        padded[z_start : z_start + planes, y_start : y_start + height, x_start : x_start + width]
        for x_start in order
    ]
    joined = jnp.concatenate(parts, axis=-1)
    return joined.reshape(planes * height * width, joined.shape[-1])


def per_device(volume, weight, cotangent):
    chans = weight.shape[1]
    planes = volume.shape[1]
    height = volume.shape[2]
    width = volume.shape[3] // chans
    cells = planes * height * width
    kern = weight.reshape(3, 3, 3, chans, chans)
    dims = ("NDHWC", "DHWIO", "NDHWC")
    same = [(0, 0), (1, 1), (1, 1)]
    extended = padded_2(volume, (("dp", 1),), 1)
    v_ext = extended.reshape(1, planes + 2, height, width, chans)
    pre = lax.conv_general_dilated(
        v_ext, kern, (1, 1, 1), same, dimension_numbers=dims, preferred_element_type=jnp.float32
    ).reshape(cells, chans)
    sig = jax.nn.sigmoid(pre)
    activation = (pre * sig).astype(jnp.bfloat16).reshape(1, planes, height, width * chans)
    delta = (
        cotangent.reshape(cells, chans).astype(jnp.float32) * sig * (1.0 + pre * (1.0 - sig))
    ).astype(jnp.bfloat16)
    v_pad = jnp.pad(v_ext, ((0, 0), (0, 0), (1, 1), (1, 1), (0, 0)))
    grads = lax.conv_general_dilated(
        v_pad,
        delta.reshape(1, planes, height, width, chans),
        (1, 1, 1),
        [(0, 0), (0, 0), (0, 0)],
        dimension_numbers=("CDHWN", "IDHWO", "NDHWC"),
        preferred_element_type=jnp.float32,
    )
    scale = 1.0 / math.sqrt(lax.axis_size("dp") * lax.axis_size("gz") * cells)
    terms = grads.transpose(1, 2, 3, 0, 4).reshape(27 * chans, chans) * scale
    reduced = sum_at_owner(terms.astype(jnp.bfloat16), "dp", 1)
    weight_grad = sum_at_owner_2(reduced, "gz", 0)
    late, _ = lax.optimization_barrier((delta, reduced))
    delta_ext = padded_2(late.reshape(1, planes, height, width * chans), (("dp", 1),), 1)
    d_ext = delta_ext.reshape(1, planes + 2, height, width, chans)
    flipped = jnp.flip(kern, (0, 1, 2)).transpose(0, 1, 2, 4, 3)
    back = lax.conv_general_dilated(
        d_ext, flipped, (1, 1, 1), same, dimension_numbers=dims, preferred_element_type=jnp.float32
    )
    input_grad = back.astype(jnp.bfloat16).reshape(1, planes, height, width * chans)
    return (activation, input_grad, weight_grad)


def solution(mesh):
    return jax.shard_map(
        per_device,
        mesh=mesh,
        in_specs=(P("gz", "dp", None, None), P(), P("gz", "dp", None, None)),
        out_specs=(P("gz", "dp", None, None), P("gz", "dp", None, None), P("gz", "dp")),
        check_vma=False,
    )
```

```python
import math

import jax
import jax.numpy as jnp
from jax import lax
from jax.sharding import PartitionSpec as P


def padded_2(block, sides, width):
    for axis, dim in sides:
        count = lax.axis_size(axis)
        forward = [(i, i + 1) for i in range(count - 1)]
        backward = [(target, source) for source, target in forward]
        low = lax.ppermute(
            lax.slice_in_dim(block, block.shape[dim] - width, None, axis=dim), axis, forward
        )
        high = lax.ppermute(lax.slice_in_dim(block, 0, width, axis=dim), axis, backward)
        block = jnp.concatenate([low, block, high], axis=dim)
    return block


def split_up(value, dim, size):
    dims = value.shape
    pieces = value.reshape(*dims[:dim], size, dims[dim] // size, *dims[dim + 1 :])
    return jnp.moveaxis(pieces, dim, 0)


def sum_at_owner(value, axis, dim):
    size = lax.axis_size(axis)
    pieces = lax.all_to_all(split_up(value, dim, size), axis, 0, 0, tiled=True)
    return jnp.sum(pieces.astype(jnp.float32), axis=0)


def sum_at_owner_2(value, axis, dim):
    pieces = split_up(value, dim, lax.axis_size(axis))
    arrived = lax.all_to_all(pieces, axis, split_axis=0, concat_axis=0, tiled=True)
    return arrived.sum(axis=0)


def strips(padded, z_start, y_start, planes, height, width, order):
    parts = [
        padded[z_start : z_start + planes, y_start : y_start + height, x_start : x_start + width]
        for x_start in order
    ]
    joined = jnp.concatenate(parts, axis=-1)
    return joined.reshape(planes * height * width, joined.shape[-1])


def per_device(volume, weight, cotangent):
    chans = weight.shape[1]
    planes = volume.shape[1]
    height = volume.shape[2]
    width = volume.shape[3] // chans
    cells = planes * height * width
    kern = weight.reshape(3, 3, 3, chans, chans)
    dims = ("NDHWC", "DHWIO", "NDHWC")
    same = [(0, 0), (1, 1), (1, 1)]
    extended = padded_2(volume, (("dp", 1),), 1)
    v_ext = extended.reshape(1, planes + 2, height, width, chans)
    pre = lax.conv_general_dilated(
        v_ext, kern, (1, 1, 1), same, dimension_numbers=dims, preferred_element_type=jnp.float32
    ).reshape(cells, chans)
    sig = jax.nn.sigmoid(pre)
    activation = (pre * sig).astype(jnp.bfloat16).reshape(1, planes, height, width * chans)
    delta = (
        cotangent.reshape(cells, chans).astype(jnp.float32) * sig * (1.0 + pre * (1.0 - sig))
    ).astype(jnp.bfloat16)
    delta_ext = padded_2(delta.reshape(1, planes, height, width * chans), (("dp", 1),), 1)
    d_ext = delta_ext.reshape(1, planes + 2, height, width, chans)
    flipped = jnp.flip(kern, (0, 1, 2)).transpose(0, 1, 2, 4, 3)
    back = lax.conv_general_dilated(
        d_ext, flipped, (1, 1, 1), same, dimension_numbers=dims, preferred_element_type=jnp.float32
    )
    input_grad = back.astype(jnp.bfloat16).reshape(1, planes, height, width * chans)
    v_pad = jnp.pad(v_ext, ((0, 0), (0, 0), (1, 1), (1, 1), (0, 0)))
    grads = lax.conv_general_dilated(
        v_pad,
        delta.reshape(1, planes, height, width, chans),
        (1, 1, 1),
        [(0, 0), (0, 0), (0, 0)],
        dimension_numbers=("CDHWN", "IDHWO", "NDHWC"),
        preferred_element_type=jnp.float32,
    )
    scale = 1.0 / math.sqrt(lax.axis_size("dp") * lax.axis_size("gz") * cells)
    terms = grads.transpose(1, 2, 3, 0, 4).reshape(27 * chans, chans) * scale
    reduced = sum_at_owner(terms.astype(jnp.bfloat16), "dp", 1)
    weight_grad = sum_at_owner(reduced.astype(jnp.bfloat16), "gz", 0)
    return (activation, input_grad, weight_grad)


def solution(mesh):
    return jax.shard_map(
        per_device,
        mesh=mesh,
        in_specs=(P("gz", "dp", None, None), P(), P("gz", "dp", None, None)),
        out_specs=(P("gz", "dp", None, None), P("gz", "dp", None, None), P("gz", "dp")),
        check_vma=False,
    )
```
